512 devices in a mesh: lat: 128 (over x, z, core), lev: 4 (over y).
Axes of the slice: x: 4, y: 4, z: 16, core: 2. Of those that a mesh axis runs over, the one named last changes fastest.
Arguments:
- fields: float32 [2, 640, 8, 2560], P(None, 'lat', 'lev'), may hold values from -6 to 6
- dep_row: int32 [640, 8, 2560], P('lat', 'lev'), may hold values from -2 to 2
- dep_col: int32 [640, 8, 2560], P('lat', 'lev'), may hold values from -4 to 4
- legendre: bfloat16 [384, 640, 384], P('lat'), may hold values from -0.25 to 0.25
- lat_weights: float32 [640], replicated, may hold values from 0.3 to 1.7
- to_modes: float32 [8, 8], replicated, may hold values from -2 to 2
- from_modes: float32 [8, 8], replicated, may hold values from -2 to 2
- mode_rates: float32 [8], replicated, may hold values from 0.1 to 10
Outputs:
- updated: float32 [2, 640, 8, 2560], P(None, 'lat', 'lev')
The draws below stay inside these ranges and needn't reach their ends.
Inputs may be any that keep to these rules, and one draw needn't show every extreme that they name: `dep_row`: departure rows lie within two latitudes of the arrival row. `dep_col`: departure columns lie within four longitudes of the arrival column.
All inputs are finite; a program needn't handle non-finite values.
Results may differ from the reference program's by a relative error of at most 0.0003.
Values sent between devices are 32-bit elements; how exact they have to be, the bound alone decides.
No kernel may reach another device: no remote copies, remote signals or barrier semaphores. Data moves between devices by JAX's collectives and lax.ppermute only.
A program may use at most 64 MiB of HBM per device.

```python
import math
import jax
import jax.numpy as jnp
from jax import lax

F = 2
NLAT = 640
NLON = 2560
TRUNC = 384
NLEV = 8


def with_ends(array, rng, low, high):
    extent = array.shape
    index_at = [jax.random.randint(jax.random.fold_in(rng, axis), (), 0, extent[axis]) for axis in range(len(extent))]
    array = array.at[tuple(index_at)].set(low)
    longest = extent.index(max(extent))
    index_at[longest] = (index_at[longest] + 1) % extent[longest]
    return array.at[tuple(index_at)].set(high)


def shard_levels(stream_key, dims, shards, smallest, largest):
    loudness, own = 1.0, jax.random.fold_in(stream_key, 6)
    for dim, parts in shards:
        draws = jnp.exp(jax.random.uniform(jax.random.fold_in(own, dim), (parts,), jnp.float32, smallest / len(shards), largest / len(shards)))
        loudness = loudness * jnp.repeat(draws, dims[dim] // parts).reshape([-1 if axis == dim else 1 for axis in range(len(dims))])
    return loudness


def centred(own_key, shape, scale, bound, cuts=(), kind=jnp.bfloat16):
    gain = shard_levels(own_key, shape, cuts, -0.22, 0.18) if cuts else 1.0
    entries = jax.random.normal(own_key, shape, jnp.float32) * scale * gain
    return jnp.minimum(jnp.maximum(entries, -bound), bound).astype(kind)


def setup_inputs(seed: int = 0) -> dict:
    arg_keys = jax.random.split(jax.random.key(seed), 9)
    return {
        "fields": centred(arg_keys[0], (F, NLAT, NLEV, NLON), 1.0, 6.0, ((1, 128), (2, 4)), jnp.float32),
        "dep_row": with_ends(jax.random.randint(arg_keys[1], (NLAT, NLEV, NLON), -2, 3), jax.random.fold_in(arg_keys[1], 1), -2, 2).astype(jnp.int32),
        "dep_col": with_ends(jax.random.randint(arg_keys[2], (NLAT, NLEV, NLON), -4, 5), jax.random.fold_in(arg_keys[2], 1), -4, 4).astype(jnp.int32),
        "legendre": centred(arg_keys[3], (TRUNC, NLAT, TRUNC), NLAT ** -0.5, 0.25, ((0, 128),)),
        "lat_weights": jnp.clip(jax.random.uniform(arg_keys[4], (NLAT,), jnp.float32, 0.3, 1.7), 0.3, 1.7),
        "to_modes": centred(arg_keys[5], (NLEV, NLEV), NLEV ** -0.5, 2.0, (), jnp.float32),
        "from_modes": centred(arg_keys[6], (NLEV, NLEV), NLEV ** -0.5, 2.0, (), jnp.float32),
        "mode_rates": jnp.clip(jnp.exp(jax.random.uniform(arg_keys[7], (NLEV,), jnp.float32, math.log(0.1), math.log(10.0))), 0.1, 10.0),
    }


stencil_weights = (-0.0625, 0.5625, 0.5625, -0.0625)
stiffness = 4.0
highest = lax.Precision.HIGHEST


def departure_interp(padded, dep_row, dep_col, row_offset):
    nfield, nrow, nlevel, nlon = padded.shape
    npoint = dep_row.shape[0]
    flattened = jnp.transpose(padded, (0, 2, 1, 3)).reshape(nfield, nlevel, nrow * nlon)
    row_base = jnp.arange(npoint, dtype=jnp.int32)[:, None, None] + row_offset - 1 + dep_row
    col_base = jnp.arange(nlon, dtype=jnp.int32)[None, None, :] + dep_col - 1
    summed = jnp.zeros((nfield, nlevel, npoint * nlon), jnp.float32)
    for row_step in range(4):
        for col_step in range(4):
            position = (row_base + row_step) * nlon + (col_base + col_step) % nlon
            position = jnp.transpose(position, (1, 0, 2)).reshape(1, nlevel, npoint * nlon).astype(jnp.int32)
            position = jnp.broadcast_to(position, (nfield, nlevel, npoint * nlon))
            picked = jnp.take_along_axis(flattened, position, axis=2)
            summed = summed + (stencil_weights[row_step] * stencil_weights[col_step]) * picked
    return jnp.transpose(summed.reshape(nfield, nlevel, npoint, nlon), (0, 2, 1, 3))


def fourier_tables(nlon, trunc):
    column = jnp.arange(nlon, dtype=jnp.int32)[:, None]
    wave = jnp.arange(trunc, dtype=jnp.int32)[None, :]
    angles = ((column * wave) % nlon).astype(jnp.float32) * jnp.float32(2.0 * math.pi / nlon)
    cosine = jnp.cos(angles)
    sine_part = jnp.sin(angles)
    forward = jnp.stack([cosine, -sine_part], 0) / jnp.float32(nlon)
    doubling = jnp.where(wave == 0, jnp.float32(1.0), jnp.float32(2.0))
    backward = jnp.stack([cosine * doubling, -sine_part * doubling], 0)
    return forward, backward


def triangle_mask(wave_first, wave_count, trunc):
    wave = wave_first + jnp.arange(wave_count, dtype=jnp.int32)
    degree = jnp.arange(trunc, dtype=jnp.int32)
    return (degree[None, :] >= wave[:, None]).astype(jnp.float32)


def damping(rates, degree_first, degree_count, trunc):
    degree = (degree_first + jnp.arange(degree_count, dtype=jnp.int32)).astype(jnp.float32)
    degree_term = degree * (degree + 1.0) / jnp.float32(trunc * (trunc + 1))
    return 1.0 / (1.0 + stiffness * rates[:, None] * degree_term[None, :])


def reference(fields, dep_row, dep_col, legendre, lat_weights, to_modes, from_modes, mode_rates):
    padded = jnp.pad(fields, ((0, 0), (4, 4), (0, 0), (0, 0)))
    advected = departure_interp(padded, dep_row, dep_col, 4)
    forward, backward = fourier_tables(NLON, TRUNC)
    coeffs = jnp.einsum("fplj,rjm->flrmp", advected, forward, precision=highest)
    basis = legendre.astype(jnp.float32) * triangle_mask(0, TRUNC, TRUNC)[:, None, :]
    spectrum = jnp.einsum("flrmp,mpn->flrmn", coeffs * lat_weights, basis, precision=highest)
    modal = jnp.einsum("kl,flrmn->fkrmn", to_modes, spectrum, precision=highest)
    scaled = modal * damping(mode_rates, 0, TRUNC, TRUNC)[None, :, None, None, :]
    solved = jnp.einsum("lk,fkrmn->flrmn", from_modes, scaled, precision=highest)
    gridded = jnp.einsum("flrmn,mpn->flrmp", solved, basis, precision=highest)
    return jnp.einsum("flrmp,rjm->fplj", gridded, backward, precision=highest)
```

```python
import math

import jax
import jax.numpy as jnp
import numpy as np
from jax import lax
from jax.sharding import Mesh
from jax.sharding import PartitionSpec as P

stencil_weights = (-0.0625, 0.5625, 0.5625, -0.0625)
stiffness = 4.0
highest = lax.Precision.HIGHEST

LAT = ("lo", "lc")


def with_halo(block, count, width):
    forward = [(i, i + 1) for i in range(count - 1)]
    backward = [(target, source) for source, target in forward]
    low = lax.ppermute(lax.slice_in_dim(block, block.shape[1] - width, None, axis=1), LAT, forward)
    high = lax.ppermute(lax.slice_in_dim(block, 0, width, axis=1), LAT, backward)
    return jnp.concatenate([low, block, high], axis=1)


def departure_interp(padded, dep_row, dep_col, row_offset):
    npoint = dep_row.shape[0]
    row_sel = dep_row[None]
    col_sel = dep_col[None]
    result = jnp.zeros((padded.shape[0], npoint, padded.shape[2], padded.shape[3]), jnp.float32)
    for col_value in range(-4, 5):
        along_lon = stencil_weights[0] * jnp.roll(padded, 1 - col_value, axis=3)
        for col_step in range(1, 4):
            along_lon = along_lon + stencil_weights[col_step] * jnp.roll(
                padded, 1 - col_value - col_step, axis=3
            )
        chosen = jnp.zeros_like(result)
        for row_value in range(-2, 3):
            first_row = row_offset + row_value - 1
            along_lat = stencil_weights[0] * along_lon[:, first_row : first_row + npoint]
            for row_step in range(1, 4):
                begin = first_row + row_step
                along_lat = (
                    along_lat + stencil_weights[row_step] * along_lon[:, begin : begin + npoint]
                )
            chosen = jnp.where(row_sel == row_value, along_lat, chosen)
        result = jnp.where(col_sel == col_value, chosen, result)
    return result


def split_factor(n):
    for b in range(int(math.isqrt(n)), 0, -1):
        if n % b == 0:
            return b
    return 1


def fourier_tables(nlon, cut_off):
    inner = split_factor(nlon)
    outer = nlon // inner
    wave = jnp.arange(cut_off, dtype=jnp.int32)[None, :]
    scale = jnp.float32(2.0 * math.pi / nlon)
    coarse = (jnp.arange(outer, dtype=jnp.int32)[:, None] * inner * wave % nlon).astype(jnp.float32) * scale
    fine = (jnp.arange(inner, dtype=jnp.int32)[:, None] * wave % nlon).astype(jnp.float32) * scale
    cos_c, sin_c = jnp.cos(coarse)[:, None, :], jnp.sin(coarse)[:, None, :]
    cos_f, sin_f = jnp.cos(fine)[None, :, :], jnp.sin(fine)[None, :, :]
    cosine = (cos_c * cos_f - sin_c * sin_f).reshape(nlon, cut_off)
    sine_part = (sin_c * cos_f + cos_c * sin_f).reshape(nlon, cut_off)
    forward = jnp.stack([cosine, -sine_part], 0) / jnp.float32(nlon)
    doubling = jnp.where(wave == 0, jnp.float32(1.0), jnp.float32(2.0))
    backward = jnp.stack([cosine * doubling, -sine_part * doubling], 0)
    return (forward, backward)


def triangle_mask(wave_first, wave_count, cut_off):
    wave = wave_first + jnp.arange(wave_count, dtype=jnp.int32)
    degree = jnp.arange(cut_off, dtype=jnp.int32)
    return (degree[None, :] >= wave[:, None]).astype(jnp.float32)


def damping(rates, degree_count, cut_off):
    degree = jnp.arange(degree_count, dtype=jnp.int32).astype(jnp.float32)
    degree_term = degree * (degree + 1.0) / jnp.float32(cut_off * (cut_off + 1))
    return 1.0 / (1.0 + stiffness * rates[:, None] * degree_term[None, :])


def make_per_device(n_lo, n_lc, n_lev):
    def per_device(fields, dep_row, dep_col, legendre, lat_weights, to_modes, from_modes, mode_rates):
        nfield, npoint, lev_dev, nlon = fields.shape
        wave_dev, nlat, cut_off = legendre.shape
        padded = with_halo(fields, n_lo * n_lc, 4)
        advected = departure_interp(padded, dep_row, dep_col, 4)
        forward, backward = fourier_tables(nlon, cut_off)
        coeffs = jnp.einsum("fplj,rjm->frlmp", advected, forward, precision=highest)
        nr = coeffs.shape[1]
        coeffs = coeffs.reshape(nfield * nr, lev_dev, cut_off, npoint)
        by_pair = lax.all_to_all(coeffs, "lev", split_axis=0, concat_axis=1, tiled=True)
        npair = by_pair.shape[0]
        nlev = by_pair.shape[1]
        staged = by_pair.reshape(npair, nlev, n_lo, n_lc, wave_dev, 1, 1, npoint)
        staged = lax.all_to_all(staged, "lc", split_axis=3, concat_axis=6, tiled=True)
        staged = lax.all_to_all(staged, "lo", split_axis=2, concat_axis=5, tiled=True)
        by_wave = staged.reshape(npair, nlev, wave_dev, nlat)
        wave_first = lax.axis_index(LAT) * wave_dev
        basis = legendre.astype(jnp.float32) * triangle_mask(wave_first, wave_dev, cut_off)[:, None, :]
        spectrum = jnp.einsum("clmp,mpn->clmn", by_wave * lat_weights, basis, precision=highest)
        modal = jnp.einsum("kl,clmn->ckmn", to_modes, spectrum, precision=highest)
        scaled = modal * damping(mode_rates, cut_off, cut_off)[None, :, None, :]
        solved = jnp.einsum("lk,ckmn->clmn", from_modes, scaled, precision=highest)
        gridded = jnp.einsum("clmn,mpn->clmp", solved, basis, precision=highest)
        staged = gridded.reshape(npair, nlev, 1, 1, wave_dev, n_lo, n_lc, npoint)
        staged = lax.all_to_all(staged, "lo", split_axis=5, concat_axis=2, tiled=True)
        staged = lax.all_to_all(staged, "lc", split_axis=6, concat_axis=3, tiled=True)
        by_lat = staged.reshape(npair, nlev, cut_off, npoint)
        by_lat = lax.all_to_all(by_lat, "lev", split_axis=1, concat_axis=0, tiled=True)
        by_lat = by_lat.reshape(nfield, nr, lev_dev, cut_off, npoint)
        return jnp.einsum("frlmp,rjm->fplj", by_lat, backward, precision=highest)

    return per_device


def solution(mesh):
    n_lat = mesh.shape["lat"]
    n_lev = mesh.shape["lev"]
    n_lc = 2 if n_lat % 2 == 0 else 1
    n_lo = n_lat // n_lc
    devices = np.asarray(mesh.devices).reshape(n_lo, n_lc, n_lev)
    staged_mesh = Mesh(devices, ("lo", "lc", "lev"))
    return jax.shard_map(
        make_per_device(n_lo, n_lc, n_lev),
        mesh=staged_mesh,
        in_specs=(
            P(None, LAT, "lev", None),
            P(LAT, "lev", None),
            P(LAT, "lev", None),
            P(LAT, None, None),
            P(),
            P(),
            P(),
            P(),
        ),
        out_specs=P(None, LAT, "lev", None),
        check_vma=False,
    )
```

```python
import math

import jax
import jax.numpy as jnp
import numpy as np
from jax import lax
from jax.sharding import Mesh
from jax.sharding import PartitionSpec as P

stencil_weights = (-0.0625, 0.5625, 0.5625, -0.0625)
stiffness = 4.0
highest = lax.Precision.HIGHEST

LAT = ("lo", "lc")


def with_halo(block, count, width):
    forward = [(i, i + 1) for i in range(count - 1)]
    backward = [(target, source) for source, target in forward]
    low = lax.ppermute(lax.slice_in_dim(block, block.shape[1] - width, None, axis=1), LAT, forward)
    high = lax.ppermute(lax.slice_in_dim(block, 0, width, axis=1), LAT, backward)
    return jnp.concatenate([low, block, high], axis=1)


def tap_weight(dep, shift):
    k = shift + 1 - dep
    outer = jnp.where((k == 0) | (k == 3), jnp.float32(stencil_weights[0]), jnp.float32(0.0))
    return jnp.where((k == 1) | (k == 2), jnp.float32(stencil_weights[1]), outer)


def departure_interp(padded, dep_row, dep_col, row_offset):
    npoint = dep_row.shape[1]
    col_shifts = range(-5, 7)
    col_weights = [tap_weight(dep_col, shift)[:, None] for shift in col_shifts]
    rolled = [jnp.roll(padded, -shift, axis=3) for shift in col_shifts]
    result = None
    for row_shift in range(-3, 5):
        first = row_offset + row_shift
        inner = None
        for weight, shifted in zip(col_weights, rolled):
            term = weight * lax.slice_in_dim(shifted, first, first + npoint, axis=2)
            inner = term if inner is None else inner + term
        term = tap_weight(dep_row, row_shift)[:, None] * inner
        result = term if result is None else result + term
    return result


def split_factor(n):
    for b in range(int(math.isqrt(n)), 0, -1):
        if n % b == 0:
            return b
    return 1


def fourier_tables(nlon, cut_off):
    inner = split_factor(nlon)
    outer = nlon // inner
    wave = jnp.arange(cut_off, dtype=jnp.int32)[None, :]
    scale = jnp.float32(2.0 * math.pi / nlon)
    coarse = (jnp.arange(outer, dtype=jnp.int32)[:, None] * inner * wave % nlon).astype(jnp.float32) * scale
    fine = (jnp.arange(inner, dtype=jnp.int32)[:, None] * wave % nlon).astype(jnp.float32) * scale
    cos_c, sin_c = jnp.cos(coarse)[:, None, :], jnp.sin(coarse)[:, None, :]
    cos_f, sin_f = jnp.cos(fine)[None, :, :], jnp.sin(fine)[None, :, :]
    cosine = (cos_c * cos_f - sin_c * sin_f).reshape(nlon, cut_off)
    sine_part = (sin_c * cos_f + cos_c * sin_f).reshape(nlon, cut_off)
    forward = jnp.stack([cosine, -sine_part], 0) / jnp.float32(nlon)
    doubling = jnp.where(wave == 0, jnp.float32(1.0), jnp.float32(2.0))
    backward = jnp.stack([cosine * doubling, -sine_part * doubling], 0)
    return (forward, backward)


def triangle_mask(wave_first, wave_count, cut_off):
    wave = wave_first + jnp.arange(wave_count, dtype=jnp.int32)
    degree = jnp.arange(cut_off, dtype=jnp.int32)
    return (degree[None, :] >= wave[:, None]).astype(jnp.float32)


def damping(rates, degree_count, cut_off):
    degree = jnp.arange(degree_count, dtype=jnp.int32).astype(jnp.float32)
    degree_term = degree * (degree + 1.0) / jnp.float32(cut_off * (cut_off + 1))
    return 1.0 / (1.0 + stiffness * rates[:, None] * degree_term[None, :])


def make_per_device(n_lo, n_lc, n_lev):
    def per_device(fields, dep_row, dep_col, legendre, lat_weights, to_modes, from_modes, mode_rates):
        nfield, npoint, lev_dev, nlon = fields.shape
        wave_dev, nlat, cut_off = legendre.shape
        padded = with_halo(fields, n_lo * n_lc, 4)
        advected = departure_interp(
            jnp.transpose(padded, (2, 0, 1, 3)),
            jnp.transpose(dep_row, (1, 0, 2)),
            jnp.transpose(dep_col, (1, 0, 2)),
            4,
        )
        forward, backward = fourier_tables(nlon, cut_off)
        nr = forward.shape[0]
        split = (n_lo, n_lc, wave_dev)
        coeffs = jnp.einsum("lfpj,rjm->mfrlp", advected, forward, precision=highest)
        coeffs = coeffs.reshape(*split, nfield, nr, lev_dev, npoint)
        coeffs = jnp.transpose(coeffs, (0, 1, 3, 4, 2, 5, 6))
        coeffs = coeffs.reshape(n_lo, n_lc * nfield * nr, wave_dev, 1, lev_dev, npoint)
        staged = lax.all_to_all(coeffs, ("lc", "lev"), split_axis=1, concat_axis=3, tiled=True)
        staged = staged.reshape(n_lo, 1, wave_dev, n_lc, n_lev, lev_dev, npoint)
        staged = lax.all_to_all(staged, "lo", split_axis=0, concat_axis=1, tiled=True)
        by_wave = staged.reshape(n_lo, wave_dev, n_lc, n_lev * lev_dev, npoint)
        wave_first = lax.axis_index(LAT) * wave_dev
        basis = legendre.astype(jnp.float32) * triangle_mask(wave_first, wave_dev, cut_off)[:, None, :]
        basis = basis.reshape(wave_dev, n_lo, n_lc, npoint, cut_off)
        weights = lat_weights.reshape(n_lo, 1, n_lc, 1, npoint)
        spectrum = jnp.einsum("awblp,wabpn->lwn", by_wave * weights, basis, precision=highest)
        modal = jnp.einsum("kl,lmn->kmn", to_modes, spectrum, precision=highest)
        scaled = modal * damping(mode_rates, cut_off, cut_off)[:, None, :]
        solved = jnp.einsum("lk,kmn->lmn", from_modes, scaled, precision=highest)
        gridded = jnp.einsum("lwn,wabpn->awblp", solved, basis, precision=highest)
        staged = gridded.reshape(n_lo, 1, wave_dev, n_lc * n_lev, 1, lev_dev, npoint)
        staged = lax.all_to_all(staged, "lo", split_axis=0, concat_axis=1, tiled=True)
        staged = lax.all_to_all(staged, ("lc", "lev"), split_axis=3, concat_axis=4, tiled=True)
        by_lat = staged.reshape(n_lo, wave_dev, n_lc, nfield, nr, lev_dev, npoint)
        by_lat = jnp.transpose(by_lat, (3, 4, 5, 6, 0, 2, 1)).reshape(nfield, nr, lev_dev, npoint, cut_off)
        return jnp.einsum("frlpm,rjm->fplj", by_lat, backward, precision=highest)

    return per_device


def solution(mesh):
    n_lat = mesh.shape["lat"]
    n_lev = mesh.shape["lev"]
    n_lc = 2 if n_lat % 2 == 0 else 1
    n_lo = n_lat // n_lc
    devices = np.asarray(mesh.devices).reshape(n_lo, n_lc, n_lev)
    staged_mesh = Mesh(devices, ("lo", "lc", "lev"))
    return jax.shard_map(
        make_per_device(n_lo, n_lc, n_lev),
        mesh=staged_mesh,
        in_specs=(
            P(None, LAT, "lev", None),
            P(LAT, "lev", None),
            P(LAT, "lev", None),
            P(LAT, None, None),
            P(),
            P(),
            P(),
            P(),
        ),
        out_specs=P(None, LAT, "lev", None),
        check_vma=False,
    )
```

```python
import math

import jax
import jax.numpy as jnp
import numpy as np
from jax import lax
from jax.experimental import pallas as pl
from jax.experimental.pallas import tpu as pltpu
from jax.sharding import Mesh
from jax.sharding import PartitionSpec as P

stencil_weights = (-0.0625, 0.5625, 0.5625, -0.0625)
stiffness = 4.0
highest = lax.Precision.HIGHEST

LAT = ("lo", "lc")


def with_halo(block, count, width):
    forward = [(i, i + 1) for i in range(count - 1)]
    backward = [(target, source) for source, target in forward]
    low = lax.ppermute(lax.slice_in_dim(block, block.shape[1] - width, None, axis=1), LAT, forward)
    high = lax.ppermute(lax.slice_in_dim(block, 0, width, axis=1), LAT, backward)
    return jnp.concatenate([low, block, high], axis=1)


def tap_weight(dep, shift):
    k = shift + 1 - dep
    outer = jnp.where((k == 0) | (k == 3), jnp.float32(stencil_weights[0]), jnp.float32(0.0))
    return jnp.where((k == 1) | (k == 2), jnp.float32(stencil_weights[1]), outer)


def departure_interp(padded, dep_row, dep_col, row_offset):
    npoint = dep_row.shape[1]
    col_shifts = range(-5, 7)
    col_weights = [tap_weight(dep_col, shift)[:, None] for shift in col_shifts]
    rolled = [jnp.roll(padded, -shift, axis=3) for shift in col_shifts]
    result = None
    for row_shift in range(-3, 5):
        first = row_offset + row_shift
        inner = None
        for weight, shifted in zip(col_weights, rolled):
            term = weight * lax.slice_in_dim(shifted, first, first + npoint, axis=2)
            inner = term if inner is None else inner + term
        term = tap_weight(dep_row, row_shift)[:, None] * inner
        result = term if result is None else result + term
    return result


def advect_kernel(padded_ref, row_ref, col_ref, out_ref, weight_ref):
    nfield = padded_ref.shape[1]
    npoint, nlon = row_ref.shape[1], row_ref.shape[2]
    dep_col = col_ref[0]
    for index, shift in enumerate(range(-5, 7)):
        weight_ref[index] = tap_weight(dep_col, shift)
    dep_row = row_ref[0]
    for field in range(nfield):
        result = None
        for row_shift in range(-3, 5):
            first = 4 + row_shift
            rows = padded_ref[0, field, first : first + npoint, :]
            inner = None
            for index, shift in enumerate(range(-5, 7)):
                rolled = pltpu.roll(rows, (-shift) % nlon, 1) if shift % nlon else rows
                term = weight_ref[index] * rolled
                inner = term if inner is None else inner + term
            term = tap_weight(dep_row, row_shift) * inner
            result = term if result is None else result + term
        out_ref[0, field] = result


def advect_kernel_call(padded, dep_row, dep_col, row_offset, interpret=False):
    nlev, nfield, nrow, nlon = padded.shape
    npoint = dep_row.shape[1]
    tall = -(-npoint // 8) * 8
    padded = jnp.pad(padded, ((0, 0), (0, 0), (0, tall + 8 - nrow), (0, 0)))
    dep_row = jnp.pad(dep_row, ((0, 0), (0, tall - npoint), (0, 0)))
    dep_col = jnp.pad(dep_col, ((0, 0), (0, tall - npoint), (0, 0)))
    out = pl.pallas_call(
        advect_kernel,
        grid=(nlev,),
        in_specs=[
            pl.BlockSpec((1, nfield, tall + 8, nlon), lambda l: (l, 0, 0, 0)),
            pl.BlockSpec((1, tall, nlon), lambda l: (l, 0, 0)),
            pl.BlockSpec((1, tall, nlon), lambda l: (l, 0, 0)),
        ],
        out_specs=pl.BlockSpec((1, nfield, tall, nlon), lambda l: (l, 0, 0, 0)),
        out_shape=jax.ShapeDtypeStruct((nlev, nfield, tall, nlon), jnp.float32),
        scratch_shapes=[pltpu.VMEM((12, tall, nlon), jnp.float32)],
        interpret=interpret,
    )(padded, dep_row, dep_col)
    return out[:, :, :npoint]


def split_factor(n):
    for b in range(int(math.isqrt(n)), 0, -1):
        if n % b == 0:
            return b
    return 1


def fourier_tables(nlon, cut_off):
    inner = split_factor(nlon)
    outer = nlon // inner
    wave = jnp.arange(cut_off, dtype=jnp.int32)[None, :]
    scale = jnp.float32(2.0 * math.pi / nlon)
    coarse = (jnp.arange(outer, dtype=jnp.int32)[:, None] * inner * wave % nlon).astype(jnp.float32) * scale
    fine = (jnp.arange(inner, dtype=jnp.int32)[:, None] * wave % nlon).astype(jnp.float32) * scale
    cos_c, sin_c = jnp.cos(coarse)[:, None, :], jnp.sin(coarse)[:, None, :]
    cos_f, sin_f = jnp.cos(fine)[None, :, :], jnp.sin(fine)[None, :, :]
    cosine = (cos_c * cos_f - sin_c * sin_f).reshape(nlon, cut_off)
    sine_part = (sin_c * cos_f + cos_c * sin_f).reshape(nlon, cut_off)
    forward = jnp.stack([cosine, -sine_part], 0) / jnp.float32(nlon)
    doubling = jnp.where(wave == 0, jnp.float32(1.0), jnp.float32(2.0))
    backward = jnp.stack([cosine * doubling, -sine_part * doubling], 0)
    return (forward, backward)


def triangle_mask(wave_first, wave_count, cut_off):
    wave = wave_first + jnp.arange(wave_count, dtype=jnp.int32)
    degree = jnp.arange(cut_off, dtype=jnp.int32)
    return (degree[None, :] >= wave[:, None]).astype(jnp.float32)


def damping(rates, degree_count, cut_off):
    degree = jnp.arange(degree_count, dtype=jnp.int32).astype(jnp.float32)
    degree_term = degree * (degree + 1.0) / jnp.float32(cut_off * (cut_off + 1))
    return 1.0 / (1.0 + stiffness * rates[:, None] * degree_term[None, :])


def make_per_device(n_lo, n_lc, n_lev):
    def per_device(fields, dep_row, dep_col, legendre, lat_weights, to_modes, from_modes, mode_rates):
        nfield, npoint, lev_dev, nlon = fields.shape
        wave_dev, nlat, cut_off = legendre.shape
        padded = with_halo(fields, n_lo * n_lc, 4)
        advected = advect_kernel_call(
            jnp.transpose(padded, (2, 0, 1, 3)),
            jnp.transpose(dep_row, (1, 0, 2)),
            jnp.transpose(dep_col, (1, 0, 2)),
            4,
        )
        forward, backward = fourier_tables(nlon, cut_off)
        nr = forward.shape[0]
        split = (n_lo, n_lc, wave_dev)
        coeffs = jnp.einsum("lfpj,rjm->mfrlp", advected, forward, precision=highest)
        coeffs = coeffs.reshape(*split, nfield, nr, lev_dev, npoint)
        coeffs = jnp.transpose(coeffs, (0, 1, 3, 4, 2, 5, 6))
        coeffs = coeffs.reshape(n_lo, n_lc * nfield * nr, wave_dev, 1, lev_dev, npoint)
        staged = lax.all_to_all(coeffs, ("lc", "lev"), split_axis=1, concat_axis=3, tiled=True)
        staged = staged.reshape(n_lo, 1, wave_dev, n_lc, n_lev, lev_dev, npoint)
        staged = lax.all_to_all(staged, "lo", split_axis=0, concat_axis=1, tiled=True)
        by_wave = staged.reshape(n_lo, wave_dev, n_lc, n_lev * lev_dev, npoint)
        wave_first = lax.axis_index(LAT) * wave_dev
        basis = legendre.astype(jnp.float32) * triangle_mask(wave_first, wave_dev, cut_off)[:, None, :]
        basis = basis.reshape(wave_dev, n_lo, n_lc, npoint, cut_off)
        weights = lat_weights.reshape(n_lo, 1, n_lc, 1, npoint)
        spectrum = jnp.einsum("awblp,wabpn->lwn", by_wave * weights, basis, precision=highest)
        modal = jnp.einsum("kl,lmn->kmn", to_modes, spectrum, precision=highest)
        scaled = modal * damping(mode_rates, cut_off, cut_off)[:, None, :]
        solved = jnp.einsum("lk,kmn->lmn", from_modes, scaled, precision=highest)
        gridded = jnp.einsum("lwn,wabpn->awblp", solved, basis, precision=highest)
        staged = gridded.reshape(n_lo, 1, wave_dev, n_lc * n_lev, 1, lev_dev, npoint)
        staged = lax.all_to_all(staged, "lo", split_axis=0, concat_axis=1, tiled=True)
        staged = lax.all_to_all(staged, ("lc", "lev"), split_axis=3, concat_axis=4, tiled=True)
        by_lat = staged.reshape(n_lo, wave_dev, n_lc, nfield, nr, lev_dev, npoint)
        by_lat = jnp.transpose(by_lat, (3, 4, 5, 6, 0, 2, 1)).reshape(nfield, nr, lev_dev, npoint, cut_off)
        return jnp.einsum("frlpm,rjm->fplj", by_lat, backward, precision=highest)

    return per_device


def solution(mesh):
    n_lat = mesh.shape["lat"]
    n_lev = mesh.shape["lev"]
    n_lc = 2 if n_lat % 2 == 0 else 1
    n_lo = n_lat // n_lc
    devices = np.asarray(mesh.devices).reshape(n_lo, n_lc, n_lev)
    staged_mesh = Mesh(devices, ("lo", "lc", "lev"))
    return jax.shard_map(
        make_per_device(n_lo, n_lc, n_lev),
        mesh=staged_mesh,
        in_specs=(
            P(None, LAT, "lev", None),
            P(LAT, "lev", None),
            P(LAT, "lev", None),
            P(LAT, None, None),
            P(),
            P(),
            P(),
            P(),
        ),
        out_specs=P(None, LAT, "lev", None),
        check_vma=False,
    )
```

```python
import math

import jax
import jax.numpy as jnp
import numpy as np
from jax import lax
from jax.experimental import pallas as pl
from jax.experimental.pallas import tpu as pltpu
from jax.sharding import Mesh
from jax.sharding import PartitionSpec as P

stencil_weights = (-0.0625, 0.5625, 0.5625, -0.0625)
stiffness = 4.0
highest = lax.Precision.HIGHEST
three_pass = lax.Precision.HIGH

LAT = ("lo", "lc")


def with_halo(block, count, width):
    forward = [(i, i + 1) for i in range(count - 1)]
    backward = [(target, source) for source, target in forward]
    low = lax.ppermute(lax.slice_in_dim(block, block.shape[1] - width, None, axis=1), LAT, forward)
    high = lax.ppermute(lax.slice_in_dim(block, 0, width, axis=1), LAT, backward)
    return jnp.concatenate([low, block, high], axis=1)


def tap_weight(dep, shift):
    k = shift + 1 - dep
    outer = jnp.where((k == 0) | (k == 3), jnp.float32(stencil_weights[0]), jnp.float32(0.0))
    return jnp.where((k == 1) | (k == 2), jnp.float32(stencil_weights[1]), outer)


def departure_interp(padded, dep_row, dep_col, row_offset):
    npoint = dep_row.shape[1]
    col_shifts = range(-5, 7)
    col_weights = [tap_weight(dep_col, shift)[:, None] for shift in col_shifts]
    rolled = [jnp.roll(padded, -shift, axis=3) for shift in col_shifts]
    result = None
    for row_shift in range(-3, 5):
        first = row_offset + row_shift
        inner = None
        for weight, shifted in zip(col_weights, rolled):
            term = weight * lax.slice_in_dim(shifted, first, first + npoint, axis=2)
            inner = term if inner is None else inner + term
        term = tap_weight(dep_row, row_shift)[:, None] * inner
        result = term if result is None else result + term
    return result


def advect_kernel(padded_ref, row_ref, col_ref, out_ref, weight_ref):
    nfield = padded_ref.shape[1]
    npoint, nlon = row_ref.shape[1], row_ref.shape[2]
    dep_col = col_ref[0]
    for index, shift in enumerate(range(-5, 7)):
        weight_ref[index] = tap_weight(dep_col, shift)
    dep_row = row_ref[0]
    for field in range(nfield):
        result = None
        for row_shift in range(-3, 5):
            first = 4 + row_shift
            rows = padded_ref[0, field, first : first + npoint, :]
            inner = None
            for index, shift in enumerate(range(-5, 7)):
                rolled = pltpu.roll(rows, (-shift) % nlon, 1) if shift % nlon else rows
                term = weight_ref[index] * rolled
                inner = term if inner is None else inner + term
            term = tap_weight(dep_row, row_shift) * inner
            result = term if result is None else result + term
        out_ref[0, field] = result


def advect_kernel_call(padded, dep_row, dep_col, row_offset, interpret=False):
    nlev, nfield, nrow, nlon = padded.shape
    npoint = dep_row.shape[1]
    tall = -(-npoint // 8) * 8
    padded = jnp.pad(padded, ((0, 0), (0, 0), (0, tall + 8 - nrow), (0, 0)))
    dep_row = jnp.pad(dep_row, ((0, 0), (0, tall - npoint), (0, 0)))
    dep_col = jnp.pad(dep_col, ((0, 0), (0, tall - npoint), (0, 0)))
    out = pl.pallas_call(
        advect_kernel,
        grid=(nlev,),
        in_specs=[
            pl.BlockSpec((1, nfield, tall + 8, nlon), lambda l: (l, 0, 0, 0)),
            pl.BlockSpec((1, tall, nlon), lambda l: (l, 0, 0)),
            pl.BlockSpec((1, tall, nlon), lambda l: (l, 0, 0)),
        ],
        out_specs=pl.BlockSpec((1, nfield, tall, nlon), lambda l: (l, 0, 0, 0)),
        out_shape=jax.ShapeDtypeStruct((nlev, nfield, tall, nlon), jnp.float32),
        scratch_shapes=[pltpu.VMEM((12, tall, nlon), jnp.float32)],
        interpret=interpret,
    )(padded, dep_row, dep_col)
    return out[:, :, :npoint]


def split_factor(n):
    for b in range(int(math.isqrt(n)), 0, -1):
        if n % b == 0:
            return b
    return 1


def fourier_tables(nlon, cut_off):
    inner = split_factor(nlon)
    outer = nlon // inner
    wave = jnp.arange(cut_off, dtype=jnp.int32)[None, :]
    scale = jnp.float32(2.0 * math.pi / nlon)
    coarse = (jnp.arange(outer, dtype=jnp.int32)[:, None] * inner * wave % nlon).astype(jnp.float32) * scale
    fine = (jnp.arange(inner, dtype=jnp.int32)[:, None] * wave % nlon).astype(jnp.float32) * scale
    cos_c, sin_c = jnp.cos(coarse)[:, None, :], jnp.sin(coarse)[:, None, :]
    cos_f, sin_f = jnp.cos(fine)[None, :, :], jnp.sin(fine)[None, :, :]
    cosine = (cos_c * cos_f - sin_c * sin_f).reshape(nlon, cut_off)
    sine_part = (sin_c * cos_f + cos_c * sin_f).reshape(nlon, cut_off)
    forward = jnp.stack([cosine, -sine_part], 0) / jnp.float32(nlon)
    doubling = jnp.where(wave == 0, jnp.float32(1.0), jnp.float32(2.0))
    backward = jnp.stack([cosine * doubling, -sine_part * doubling], 0)
    return (forward, backward)


def triangle_mask(wave_first, wave_count, cut_off):
    wave = wave_first + jnp.arange(wave_count, dtype=jnp.int32)
    degree = jnp.arange(cut_off, dtype=jnp.int32)
    return (degree[None, :] >= wave[:, None]).astype(jnp.float32)


def damping(rates, degree_count, cut_off):
    degree = jnp.arange(degree_count, dtype=jnp.int32).astype(jnp.float32)
    degree_term = degree * (degree + 1.0) / jnp.float32(cut_off * (cut_off + 1))
    return 1.0 / (1.0 + stiffness * rates[:, None] * degree_term[None, :])


def make_per_device(n_lo, n_lc, n_lev):
    def per_device(fields, dep_row, dep_col, legendre, lat_weights, to_modes, from_modes, mode_rates):
        nfield, npoint, lev_dev, nlon = fields.shape
        wave_dev, nlat, cut_off = legendre.shape
        padded = with_halo(fields, n_lo * n_lc, 4)
        advected = advect_kernel_call(
            jnp.transpose(padded, (2, 0, 1, 3)),
            jnp.transpose(dep_row, (1, 0, 2)),
            jnp.transpose(dep_col, (1, 0, 2)),
            4,
        )
        forward, backward = fourier_tables(nlon, cut_off)
        nr = forward.shape[0]
        split = (n_lo, n_lc, wave_dev)
        coeffs = jnp.einsum("lfpj,rjm->mfrlp", advected, forward, precision=three_pass)
        coeffs = coeffs.reshape(*split, nfield, nr, lev_dev, npoint)
        coeffs = jnp.transpose(coeffs, (0, 1, 3, 4, 2, 5, 6))
        coeffs = coeffs.reshape(n_lo, n_lc * nfield * nr, wave_dev, 1, lev_dev, npoint)
        staged = lax.all_to_all(coeffs, ("lc", "lev"), split_axis=1, concat_axis=3, tiled=True)
        staged = staged.reshape(n_lo, 1, wave_dev, n_lc, n_lev, lev_dev, npoint)
        staged = lax.all_to_all(staged, "lo", split_axis=0, concat_axis=1, tiled=True)
        by_wave = staged.reshape(n_lo, wave_dev, n_lc, n_lev * lev_dev, npoint)
        wave_first = lax.axis_index(LAT) * wave_dev
        basis = legendre.astype(jnp.float32) * triangle_mask(wave_first, wave_dev, cut_off)[:, None, :]
        basis = basis.reshape(wave_dev, n_lo, n_lc, npoint, cut_off)
        weights = lat_weights.reshape(n_lo, 1, n_lc, 1, npoint)
        spectrum = jnp.einsum("awblp,wabpn->lwn", by_wave * weights, basis, precision=three_pass)
        modal = jnp.einsum("kl,lmn->kmn", to_modes, spectrum, precision=highest)
        scaled = modal * damping(mode_rates, cut_off, cut_off)[:, None, :]
        solved = jnp.einsum("lk,kmn->lmn", from_modes, scaled, precision=highest)
        gridded = jnp.einsum("lwn,wabpn->awblp", solved, basis, precision=three_pass)
        staged = gridded.reshape(n_lo, 1, wave_dev, n_lc * n_lev, 1, lev_dev, npoint)
        staged = lax.all_to_all(staged, "lo", split_axis=0, concat_axis=1, tiled=True)
        staged = lax.all_to_all(staged, ("lc", "lev"), split_axis=3, concat_axis=4, tiled=True)
        by_lat = staged.reshape(n_lo, wave_dev, n_lc, nfield, nr, lev_dev, npoint)
        by_lat = jnp.transpose(by_lat, (3, 4, 5, 6, 0, 2, 1)).reshape(nfield, nr, lev_dev, npoint, cut_off)
        return jnp.einsum("frlpm,rjm->fplj", by_lat, backward, precision=three_pass)

    return per_device


def solution(mesh):
    n_lat = mesh.shape["lat"]
    n_lev = mesh.shape["lev"]
    n_lc = 2 if n_lat % 2 == 0 else 1
    n_lo = n_lat // n_lc
    devices = np.asarray(mesh.devices).reshape(n_lo, n_lc, n_lev)
    staged_mesh = Mesh(devices, ("lo", "lc", "lev"))
    return jax.shard_map(
        make_per_device(n_lo, n_lc, n_lev),
        mesh=staged_mesh,
        in_specs=(
            P(None, LAT, "lev", None),
            P(LAT, "lev", None),
            P(LAT, "lev", None),
            P(LAT, None, None),
            P(),
            P(),
            P(),
            P(),
        ),
        out_specs=P(None, LAT, "lev", None),
        check_vma=False,
    )
```

```python
import math

import jax
import jax.numpy as jnp
import numpy as np
from jax import lax
from jax.experimental import pallas as pl
from jax.experimental.pallas import tpu as pltpu
from jax.sharding import Mesh
from jax.sharding import PartitionSpec as P

stencil_weights = (-0.0625, 0.5625, 0.5625, -0.0625)
stiffness = 4.0
highest = lax.Precision.HIGHEST
three_pass = lax.Precision.HIGH

LAT = ("lo", "lc")


def with_halo(block, count, width):
    forward = [(i, i + 1) for i in range(count - 1)]
    backward = [(target, source) for source, target in forward]
    low = lax.ppermute(lax.slice_in_dim(block, block.shape[1] - width, None, axis=1), LAT, forward)
    high = lax.ppermute(lax.slice_in_dim(block, 0, width, axis=1), LAT, backward)
    return jnp.concatenate([low, block, high], axis=1)


def tap_weight(dep, shift):
    k = shift + 1 - dep
    outer = jnp.where((k == 0) | (k == 3), jnp.float32(stencil_weights[0]), jnp.float32(0.0))
    return jnp.where((k == 1) | (k == 2), jnp.float32(stencil_weights[1]), outer)


def departure_interp(padded, dep_row, dep_col, row_offset):
    npoint = dep_row.shape[1]
    col_shifts = range(-5, 7)
    col_weights = [tap_weight(dep_col, shift)[:, None] for shift in col_shifts]
    rolled = [jnp.roll(padded, -shift, axis=3) for shift in col_shifts]
    result = None
    for row_shift in range(-3, 5):
        first = row_offset + row_shift
        inner = None
        for weight, shifted in zip(col_weights, rolled):
            term = weight * lax.slice_in_dim(shifted, first, first + npoint, axis=2)
            inner = term if inner is None else inner + term
        term = tap_weight(dep_row, row_shift)[:, None] * inner
        result = term if result is None else result + term
    return result


def advect_kernel(padded_ref, row_ref, col_ref, out_ref, weight_ref):
    nfield = padded_ref.shape[1]
    npoint, nlon = row_ref.shape[1], row_ref.shape[2]
    dep_col = col_ref[0]
    for index, shift in enumerate(range(-5, 7)):
        weight_ref[index] = tap_weight(dep_col, shift)
    dep_row = row_ref[0]
    for field in range(nfield):
        result = None
        for row_shift in range(-3, 5):
            first = 4 + row_shift
            rows = padded_ref[0, field, first : first + npoint, :]
            inner = None
            for index, shift in enumerate(range(-5, 7)):
                rolled = pltpu.roll(rows, (-shift) % nlon, 1) if shift % nlon else rows
                term = weight_ref[index] * rolled
                inner = term if inner is None else inner + term
            term = tap_weight(dep_row, row_shift) * inner
            result = term if result is None else result + term
        out_ref[0, field] = result


def advect_kernel_call(padded, dep_row, dep_col, row_offset, interpret=False):
    nlev, nfield, nrow, nlon = padded.shape
    npoint = dep_row.shape[1]
    tall = -(-npoint // 8) * 8
    padded = jnp.pad(padded, ((0, 0), (0, 0), (0, tall + 8 - nrow), (0, 0)))
    dep_row = jnp.pad(dep_row, ((0, 0), (0, tall - npoint), (0, 0)))
    dep_col = jnp.pad(dep_col, ((0, 0), (0, tall - npoint), (0, 0)))
    out = pl.pallas_call(
        advect_kernel,
        grid=(nlev,),
        in_specs=[
            pl.BlockSpec((1, nfield, tall + 8, nlon), lambda l: (l, 0, 0, 0)),
            pl.BlockSpec((1, tall, nlon), lambda l: (l, 0, 0)),
            pl.BlockSpec((1, tall, nlon), lambda l: (l, 0, 0)),
        ],
        out_specs=pl.BlockSpec((1, nfield, tall, nlon), lambda l: (l, 0, 0, 0)),
        out_shape=jax.ShapeDtypeStruct((nlev, nfield, tall, nlon), jnp.float32),
        scratch_shapes=[pltpu.VMEM((12, tall, nlon), jnp.float32)],
        interpret=interpret,
    )(padded, dep_row, dep_col)
    return out[:, :, :npoint]


def split_factor(n):
    for b in range(int(math.isqrt(n)), 0, -1):
        if n % b == 0:
            return b
    return 1


def fourier_tables(nlon, cut_off):
    inner = split_factor(nlon)
    outer = nlon // inner
    wave = jnp.arange(cut_off, dtype=jnp.int32)[None, :]
    scale = jnp.float32(2.0 * math.pi / nlon)
    coarse = (jnp.arange(outer, dtype=jnp.int32)[:, None] * inner * wave % nlon).astype(jnp.float32) * scale
    fine = (jnp.arange(inner, dtype=jnp.int32)[:, None] * wave % nlon).astype(jnp.float32) * scale
    cos_c, sin_c = jnp.cos(coarse)[:, None, :], jnp.sin(coarse)[:, None, :]
    cos_f, sin_f = jnp.cos(fine)[None, :, :], jnp.sin(fine)[None, :, :]
    cosine = (cos_c * cos_f - sin_c * sin_f).reshape(nlon, cut_off)
    sine_part = (sin_c * cos_f + cos_c * sin_f).reshape(nlon, cut_off)
    table = jnp.stack([cosine, -sine_part], 0)
    doubling = jnp.where(wave == 0, jnp.float32(1.0), jnp.float32(2.0))
    return (table, doubling)


def triangle_mask(wave_first, wave_count, cut_off):
    wave = wave_first + jnp.arange(wave_count, dtype=jnp.int32)
    degree = jnp.arange(cut_off, dtype=jnp.int32)
    return (degree[None, :] >= wave[:, None]).astype(jnp.float32)


def damping(rates, degree_count, cut_off):
    degree = jnp.arange(degree_count, dtype=jnp.int32).astype(jnp.float32)
    degree_term = degree * (degree + 1.0) / jnp.float32(cut_off * (cut_off + 1))
    return 1.0 / (1.0 + stiffness * rates[:, None] * degree_term[None, :])


def make_per_device(n_lo, n_lc, n_lev):
    def per_device(fields, dep_row, dep_col, legendre, lat_weights, to_modes, from_modes, mode_rates):
        nfield, npoint, lev_dev, nlon = fields.shape
        wave_dev, nlat, cut_off = legendre.shape
        padded = with_halo(fields, n_lo * n_lc, 4)
        advected = advect_kernel_call(
            jnp.transpose(padded, (2, 0, 1, 3)),
            jnp.transpose(dep_row, (1, 0, 2)),
            jnp.transpose(dep_col, (1, 0, 2)),
            4,
        )
        table, doubling = fourier_tables(nlon, cut_off)
        nr = table.shape[0]
        split = (n_lo, n_lc, wave_dev)
        coeffs = jnp.einsum("lfpj,rjm->mfrlp", advected, table, precision=three_pass) / jnp.float32(nlon)
        coeffs = coeffs.reshape(*split, nfield, nr, lev_dev, npoint)
        coeffs = jnp.transpose(coeffs, (0, 1, 3, 4, 2, 5, 6))
        coeffs = coeffs.reshape(n_lo, n_lc * nfield * nr, wave_dev, 1, lev_dev, npoint)
        staged = lax.all_to_all(coeffs, ("lc", "lev"), split_axis=1, concat_axis=3, tiled=True)
        staged = staged.reshape(n_lo, 1, wave_dev, n_lc, n_lev, lev_dev, npoint)
        staged = lax.all_to_all(staged, "lo", split_axis=0, concat_axis=1, tiled=True)
        by_wave = staged.reshape(n_lo, wave_dev, n_lc, n_lev * lev_dev, npoint)
        wave_first = lax.axis_index(LAT) * wave_dev
        basis = legendre.astype(jnp.float32) * triangle_mask(wave_first, wave_dev, cut_off)[:, None, :]
        basis = basis.reshape(wave_dev, n_lo, n_lc, npoint, cut_off)
        weights = lat_weights.reshape(n_lo, 1, n_lc, 1, npoint)
        spectrum = jnp.einsum("awblp,wabpn->lwn", by_wave * weights, basis, precision=three_pass)
        modal = jnp.einsum("kl,lmn->kmn", to_modes, spectrum, precision=highest)
        scaled = modal * damping(mode_rates, cut_off, cut_off)[:, None, :]
        solved = jnp.einsum("lk,kmn->lmn", from_modes, scaled, precision=highest)
        gridded = jnp.einsum("lwn,wabpn->awblp", solved, basis, precision=three_pass)
        staged = gridded.reshape(n_lo, 1, wave_dev, n_lc * n_lev, 1, lev_dev, npoint)
        staged = lax.all_to_all(staged, "lo", split_axis=0, concat_axis=1, tiled=True)
        staged = lax.all_to_all(staged, ("lc", "lev"), split_axis=3, concat_axis=4, tiled=True)
        by_lat = staged.reshape(n_lo, wave_dev, n_lc, nfield, nr, lev_dev, npoint)
        by_lat = jnp.transpose(by_lat, (3, 4, 5, 6, 0, 2, 1)).reshape(nfield, nr, lev_dev, npoint, cut_off)
        return jnp.einsum("frlpm,rjm->fplj", by_lat * doubling, table, precision=three_pass)

    return per_device


def solution(mesh):
    n_lat = mesh.shape["lat"]
    n_lev = mesh.shape["lev"]
    n_lc = 2 if n_lat % 2 == 0 else 1
    n_lo = n_lat // n_lc
    devices = np.asarray(mesh.devices).reshape(n_lo, n_lc, n_lev)
    staged_mesh = Mesh(devices, ("lo", "lc", "lev"))
    return jax.shard_map(
        make_per_device(n_lo, n_lc, n_lev),
        mesh=staged_mesh,
        in_specs=(
            P(None, LAT, "lev", None),
            P(LAT, "lev", None),
            P(LAT, "lev", None),
            P(LAT, None, None),
            P(),
            P(),
            P(),
            P(),
        ),
        out_specs=P(None, LAT, "lev", None),
        check_vma=False,
    )
```

```python
import math

import jax
import jax.numpy as jnp
import numpy as np
from jax import lax
from jax.experimental import pallas as pl
from jax.experimental.pallas import tpu as pltpu
from jax.sharding import Mesh
from jax.sharding import PartitionSpec as P

stencil_weights = (-0.0625, 0.5625, 0.5625, -0.0625)
stiffness = 4.0
highest = lax.Precision.HIGHEST
three_pass = lax.Precision.HIGH

LAT = ("lo", "lc")


def with_halo(block, count, width):
    forward = [(i, i + 1) for i in range(count - 1)]
    backward = [(target, source) for source, target in forward]
    low = lax.ppermute(lax.slice_in_dim(block, block.shape[1] - width, None, axis=1), LAT, forward)
    high = lax.ppermute(lax.slice_in_dim(block, 0, width, axis=1), LAT, backward)
    return jnp.concatenate([low, block, high], axis=1)


def tap_weight(dep, shift):
    k = shift + 1 - dep
    outer = jnp.where((k == 0) | (k == 3), jnp.float32(stencil_weights[0]), jnp.float32(0.0))
    return jnp.where((k == 1) | (k == 2), jnp.float32(stencil_weights[1]), outer)


def departure_interp(padded, dep_row, dep_col, row_offset):
    npoint = dep_row.shape[1]
    col_shifts = range(-5, 7)
    col_weights = [tap_weight(dep_col, shift)[:, None] for shift in col_shifts]
    rolled = [jnp.roll(padded, -shift, axis=3) for shift in col_shifts]
    result = None
    for row_shift in range(-3, 5):
        first = row_offset + row_shift
        inner = None
        for weight, shifted in zip(col_weights, rolled):
            term = weight * lax.slice_in_dim(shifted, first, first + npoint, axis=2)
            inner = term if inner is None else inner + term
        term = tap_weight(dep_row, row_shift)[:, None] * inner
        result = term if result is None else result + term
    return result


def advect_kernel(padded_ref, row_ref, col_ref, out_ref, weight_ref, rolled_ref):
    nfield = padded_ref.shape[1]
    npoint, nlon = row_ref.shape[1], row_ref.shape[2]
    dep_col = col_ref[0]
    for index, shift in enumerate(range(-5, 7)):
        weight_ref[index] = tap_weight(dep_col, shift)
    dep_row = row_ref[0]
    for field in range(nfield):
        block = padded_ref[0, field]
        for index, shift in enumerate(range(-5, 7)):
            rolled_ref[index] = pltpu.roll(block, (-shift) % nlon, 1) if shift % nlon else block
        result = None
        for row_shift in range(-3, 5):
            first = 4 + row_shift
            inner = None
            for index in range(12):
                term = weight_ref[index] * rolled_ref[index, first : first + npoint, :]
                inner = term if inner is None else inner + term
            term = tap_weight(dep_row, row_shift) * inner
            result = term if result is None else result + term
        out_ref[0, field] = result


def advect_kernel_call(padded, dep_row, dep_col, row_offset, interpret=False):
    nlev, nfield, nrow, nlon = padded.shape
    npoint = dep_row.shape[1]
    tall = -(-npoint // 8) * 8
    padded = jnp.pad(padded, ((0, 0), (0, 0), (0, tall + 8 - nrow), (0, 0)))
    dep_row = jnp.pad(dep_row, ((0, 0), (0, tall - npoint), (0, 0)))
    dep_col = jnp.pad(dep_col, ((0, 0), (0, tall - npoint), (0, 0)))
    out = pl.pallas_call(
        advect_kernel,
        grid=(nlev,),
        in_specs=[
            pl.BlockSpec((1, nfield, tall + 8, nlon), lambda l: (l, 0, 0, 0)),
            pl.BlockSpec((1, tall, nlon), lambda l: (l, 0, 0)),
            pl.BlockSpec((1, tall, nlon), lambda l: (l, 0, 0)),
        ],
        out_specs=pl.BlockSpec((1, nfield, tall, nlon), lambda l: (l, 0, 0, 0)),
        out_shape=jax.ShapeDtypeStruct((nlev, nfield, tall, nlon), jnp.float32),
        scratch_shapes=[pltpu.VMEM((12, tall, nlon), jnp.float32), pltpu.VMEM((12, tall + 8, nlon), jnp.float32)],
        interpret=interpret,
    )(padded, dep_row, dep_col)
    return out[:, :, :npoint]


def split_factor(n):
    for b in range(int(math.isqrt(n)), 0, -1):
        if n % b == 0:
            return b
    return 1


def fourier_tables(nlon, cut_off):
    inner = split_factor(nlon)
    outer = nlon // inner
    wave = jnp.arange(cut_off, dtype=jnp.int32)[None, :]
    scale = jnp.float32(2.0 * math.pi / nlon)
    coarse = (jnp.arange(outer, dtype=jnp.int32)[:, None] * inner * wave % nlon).astype(jnp.float32) * scale
    fine = (jnp.arange(inner, dtype=jnp.int32)[:, None] * wave % nlon).astype(jnp.float32) * scale
    cos_c, sin_c = jnp.cos(coarse)[:, None, :], jnp.sin(coarse)[:, None, :]
    cos_f, sin_f = jnp.cos(fine)[None, :, :], jnp.sin(fine)[None, :, :]
    cosine = (cos_c * cos_f - sin_c * sin_f).reshape(nlon, cut_off)
    sine_part = (sin_c * cos_f + cos_c * sin_f).reshape(nlon, cut_off)
    table = jnp.stack([cosine, -sine_part], 0)
    doubling = jnp.where(wave == 0, jnp.float32(1.0), jnp.float32(2.0))
    return (table, doubling)


def triangle_mask(wave_first, wave_count, cut_off):
    wave = wave_first + jnp.arange(wave_count, dtype=jnp.int32)
    degree = jnp.arange(cut_off, dtype=jnp.int32)
    return (degree[None, :] >= wave[:, None]).astype(jnp.float32)


def damping(rates, degree_count, cut_off):
    degree = jnp.arange(degree_count, dtype=jnp.int32).astype(jnp.float32)
    degree_term = degree * (degree + 1.0) / jnp.float32(cut_off * (cut_off + 1))
    return 1.0 / (1.0 + stiffness * rates[:, None] * degree_term[None, :])


def make_per_device(n_lo, n_lc, n_lev):
    def per_device(fields, dep_row, dep_col, legendre, lat_weights, to_modes, from_modes, mode_rates):
        nfield, npoint, lev_dev, nlon = fields.shape
        wave_dev, nlat, cut_off = legendre.shape
        padded = with_halo(fields, n_lo * n_lc, 4)
        advected = advect_kernel_call(
            jnp.transpose(padded, (2, 0, 1, 3)),
            jnp.transpose(dep_row, (1, 0, 2)),
            jnp.transpose(dep_col, (1, 0, 2)),
            4,
        )
        table, doubling = fourier_tables(nlon, cut_off)
        nr = table.shape[0]
        split = (n_lo, n_lc, wave_dev)
        coeffs = jnp.einsum("lfpj,rjm->mfrlp", advected, table, precision=three_pass) / jnp.float32(nlon)
        coeffs = coeffs.reshape(*split, nfield, nr, lev_dev, npoint)
        coeffs = jnp.transpose(coeffs, (0, 1, 3, 4, 2, 5, 6))
        coeffs = coeffs.reshape(n_lo, n_lc * nfield * nr, wave_dev, 1, lev_dev, npoint)
        staged = lax.all_to_all(coeffs, ("lc", "lev"), split_axis=1, concat_axis=3, tiled=True)
        staged = staged.reshape(n_lo, 1, wave_dev, n_lc, n_lev, lev_dev, npoint)
        staged = lax.all_to_all(staged, "lo", split_axis=0, concat_axis=1, tiled=True)
        by_wave = staged.reshape(n_lo, wave_dev, n_lc, n_lev * lev_dev, npoint)
        wave_first = lax.axis_index(LAT) * wave_dev
        basis = legendre.astype(jnp.float32) * triangle_mask(wave_first, wave_dev, cut_off)[:, None, :]
        basis = basis.reshape(wave_dev, n_lo, n_lc, npoint, cut_off)
        weights = lat_weights.reshape(n_lo, 1, n_lc, 1, npoint)
        spectrum = jnp.einsum("awblp,wabpn->lwn", by_wave * weights, basis, precision=three_pass)
        modal = jnp.einsum("kl,lmn->kmn", to_modes, spectrum, precision=highest)
        scaled = modal * damping(mode_rates, cut_off, cut_off)[:, None, :]
        solved = jnp.einsum("lk,kmn->lmn", from_modes, scaled, precision=highest)
        gridded = jnp.einsum("lwn,wabpn->awblp", solved, basis, precision=three_pass)
        staged = gridded.reshape(n_lo, 1, wave_dev, n_lc * n_lev, 1, lev_dev, npoint)
        staged = lax.all_to_all(staged, "lo", split_axis=0, concat_axis=1, tiled=True)
        staged = lax.all_to_all(staged, ("lc", "lev"), split_axis=3, concat_axis=4, tiled=True)
        by_lat = staged.reshape(n_lo, wave_dev, n_lc, nfield, nr, lev_dev, npoint)
        by_lat = jnp.transpose(by_lat, (3, 4, 5, 6, 0, 2, 1)).reshape(nfield, nr, lev_dev, npoint, cut_off)
        return jnp.einsum("frlpm,rjm->fplj", by_lat * doubling, table, precision=three_pass)

    return per_device


def solution(mesh):
    n_lat = mesh.shape["lat"]
    n_lev = mesh.shape["lev"]
    n_lc = 2 if n_lat % 2 == 0 else 1
    n_lo = n_lat // n_lc
    devices = np.asarray(mesh.devices).reshape(n_lo, n_lc, n_lev)
    staged_mesh = Mesh(devices, ("lo", "lc", "lev"))
    return jax.shard_map(
        make_per_device(n_lo, n_lc, n_lev),
        mesh=staged_mesh,
        in_specs=(
            P(None, LAT, "lev", None),
            P(LAT, "lev", None),
            P(LAT, "lev", None),
            P(LAT, None, None),
            P(),
            P(),
            P(),
            P(),
        ),
        out_specs=P(None, LAT, "lev", None),
        check_vma=False,
    )
```

```python
import math

import jax
import jax.numpy as jnp
import numpy as np
from jax import lax
from jax.experimental import pallas as pl
from jax.experimental.pallas import tpu as pltpu
from jax.sharding import Mesh
from jax.sharding import PartitionSpec as P

stencil_weights = (-0.0625, 0.5625, 0.5625, -0.0625)
stiffness = 4.0
highest = lax.Precision.HIGHEST
three_pass = lax.Precision.HIGH

LAT = ("lo", "lc")


def with_halo(block, count, width):
    forward = [(i, i + 1) for i in range(count - 1)]
    backward = [(target, source) for source, target in forward]
    low = lax.ppermute(lax.slice_in_dim(block, block.shape[1] - width, None, axis=1), LAT, forward)
    high = lax.ppermute(lax.slice_in_dim(block, 0, width, axis=1), LAT, backward)
    return jnp.concatenate([low, block, high], axis=1)


def tap_weight(dep, shift):
    k = shift + 1 - dep
    outer = jnp.where((k == 0) | (k == 3), jnp.float32(stencil_weights[0]), jnp.float32(0.0))
    return jnp.where((k == 1) | (k == 2), jnp.float32(stencil_weights[1]), outer)


def departure_interp(padded, dep_row, dep_col, row_offset):
    npoint = dep_row.shape[1]
    col_shifts = range(-5, 7)
    col_weights = [tap_weight(dep_col, shift)[:, None] for shift in col_shifts]
    rolled = [jnp.roll(padded, -shift, axis=3) for shift in col_shifts]
    result = None
    for row_shift in range(-3, 5):
        first = row_offset + row_shift
        inner = None
        for weight, shifted in zip(col_weights, rolled):
            term = weight * lax.slice_in_dim(shifted, first, first + npoint, axis=2)
            inner = term if inner is None else inner + term
        term = tap_weight(dep_row, row_shift)[:, None] * inner
        result = term if result is None else result + term
    return result


def advect_kernel(padded_ref, row_ref, col_ref, out_ref, weight_ref, rolled_ref):
    nfield, nrow = padded_ref.shape[1], padded_ref.shape[2]
    npoint, nlon = row_ref.shape[1], row_ref.shape[2]
    tall = weight_ref.shape[1]
    dep_col = col_ref[0]
    for index, shift in enumerate(range(-5, 7)):
        weight_ref[index, :npoint] = tap_weight(dep_col, shift)
    dep_row = row_ref[0]
    row_weights = [tap_weight(dep_row, row_shift) for row_shift in range(-3, 5)]
    for field in range(nfield):
        block = padded_ref[0, field]
        for index, shift in enumerate(range(-5, 7)):
            rolled_ref[index, :nrow] = pltpu.roll(block, (-shift) % nlon, 1) if shift % nlon else block
        result = None
        for count, row_shift in enumerate(range(-3, 5)):
            first = 4 + row_shift
            inner = None
            for index in range(12):
                term = weight_ref[index] * rolled_ref[index, first : first + tall, :]
                inner = term if inner is None else inner + term
            term = row_weights[count] * inner[:npoint]
            result = term if result is None else result + term
        out_ref[0, field] = result


def advect_kernel_call(padded, dep_row, dep_col, row_offset, interpret=False):
    nlev, nfield, nrow, nlon = padded.shape
    npoint = dep_row.shape[1]
    tall = -(-npoint // 8) * 8
    return pl.pallas_call(
        advect_kernel,
        grid=(nlev,),
        in_specs=[
            pl.BlockSpec((1, nfield, nrow, nlon), lambda l: (l, 0, 0, 0)),
            pl.BlockSpec((1, npoint, nlon), lambda l: (l, 0, 0)),
            pl.BlockSpec((1, npoint, nlon), lambda l: (l, 0, 0)),
        ],
        out_specs=pl.BlockSpec((1, nfield, npoint, nlon), lambda l: (l, 0, 0, 0)),
        out_shape=jax.ShapeDtypeStruct((nlev, nfield, npoint, nlon), jnp.float32),
        scratch_shapes=[pltpu.VMEM((12, tall, nlon), jnp.float32), pltpu.VMEM((12, tall + 8, nlon), jnp.float32)],
        interpret=interpret,
    )(padded, dep_row, dep_col)


def split_factor(n):
    for b in range(int(math.isqrt(n)), 0, -1):
        if n % b == 0:
            return b
    return 1


def fourier_tables(nlon, cut_off):
    inner = split_factor(nlon)
    outer = nlon // inner
    wave = jnp.arange(cut_off, dtype=jnp.int32)[None, :]
    scale = jnp.float32(2.0 * math.pi / nlon)
    coarse = (jnp.arange(outer, dtype=jnp.int32)[:, None] * inner * wave % nlon).astype(jnp.float32) * scale
    fine = (jnp.arange(inner, dtype=jnp.int32)[:, None] * wave % nlon).astype(jnp.float32) * scale
    cos_c, sin_c = jnp.cos(coarse)[:, None, :], jnp.sin(coarse)[:, None, :]
    cos_f, sin_f = jnp.cos(fine)[None, :, :], jnp.sin(fine)[None, :, :]
    cosine = (cos_c * cos_f - sin_c * sin_f).reshape(nlon, cut_off)
    sine_part = (sin_c * cos_f + cos_c * sin_f).reshape(nlon, cut_off)
    table = jnp.stack([cosine, -sine_part], 0)
    doubling = jnp.where(wave == 0, jnp.float32(1.0), jnp.float32(2.0))
    return (table, doubling)


def triangle_mask(wave_first, wave_count, cut_off):
    wave = wave_first + jnp.arange(wave_count, dtype=jnp.int32)
    degree = jnp.arange(cut_off, dtype=jnp.int32)
    return (degree[None, :] >= wave[:, None]).astype(jnp.float32)


def damping(rates, degree_count, cut_off):
    degree = jnp.arange(degree_count, dtype=jnp.int32).astype(jnp.float32)
    degree_term = degree * (degree + 1.0) / jnp.float32(cut_off * (cut_off + 1))
    return 1.0 / (1.0 + stiffness * rates[:, None] * degree_term[None, :])


def make_per_device(n_lo, n_lc, n_lev):
    def per_device(fields, dep_row, dep_col, legendre, lat_weights, to_modes, from_modes, mode_rates):
        nfield, npoint, lev_dev, nlon = fields.shape
        wave_dev, nlat, cut_off = legendre.shape
        padded = with_halo(fields, n_lo * n_lc, 4)
        advected = advect_kernel_call(
            jnp.transpose(padded, (2, 0, 1, 3)),
            jnp.transpose(dep_row, (1, 0, 2)),
            jnp.transpose(dep_col, (1, 0, 2)),
            4,
        )
        table, doubling = fourier_tables(nlon, cut_off)
        nr = table.shape[0]
        split = (n_lo, n_lc, wave_dev)
        coeffs = jnp.einsum("lfpj,rjm->mfrlp", advected, table, precision=three_pass) / jnp.float32(nlon)
        coeffs = coeffs.reshape(*split, nfield, nr, lev_dev, npoint)
        coeffs = jnp.transpose(coeffs, (0, 1, 3, 4, 2, 5, 6))
        coeffs = coeffs.reshape(n_lo, n_lc * nfield * nr, wave_dev, 1, lev_dev, npoint)
        staged = lax.all_to_all(coeffs, ("lc", "lev"), split_axis=1, concat_axis=3, tiled=True)
        staged = staged.reshape(n_lo, 1, wave_dev, n_lc, n_lev, lev_dev, npoint)
        staged = lax.all_to_all(staged, "lo", split_axis=0, concat_axis=1, tiled=True)
        by_wave = staged.reshape(n_lo, wave_dev, n_lc, n_lev * lev_dev, npoint)
        wave_first = lax.axis_index(LAT) * wave_dev
        basis = legendre.astype(jnp.float32) * triangle_mask(wave_first, wave_dev, cut_off)[:, None, :]
        basis = basis.reshape(wave_dev, n_lo, n_lc, npoint, cut_off)
        weights = lat_weights.reshape(n_lo, 1, n_lc, 1, npoint)
        spectrum = jnp.einsum("awblp,wabpn->lwn", by_wave * weights, basis, precision=three_pass)
        modal = jnp.einsum("kl,lmn->kmn", to_modes, spectrum, precision=highest)
        scaled = modal * damping(mode_rates, cut_off, cut_off)[:, None, :]
        solved = jnp.einsum("lk,kmn->lmn", from_modes, scaled, precision=highest)
        gridded = jnp.einsum("lwn,wabpn->awblp", solved, basis, precision=three_pass)
        staged = gridded.reshape(n_lo, 1, wave_dev, n_lc * n_lev, 1, lev_dev, npoint)
        staged = lax.all_to_all(staged, "lo", split_axis=0, concat_axis=1, tiled=True)
        staged = lax.all_to_all(staged, ("lc", "lev"), split_axis=3, concat_axis=4, tiled=True)
        by_lat = staged.reshape(n_lo, wave_dev, n_lc, nfield, nr, lev_dev, npoint)
        by_lat = jnp.transpose(by_lat, (3, 4, 5, 6, 0, 2, 1)).reshape(nfield, nr, lev_dev, npoint, cut_off)
        return jnp.einsum("frlpm,rjm->fplj", by_lat * doubling, table, precision=three_pass)

    return per_device


def solution(mesh):
    n_lat = mesh.shape["lat"]
    n_lev = mesh.shape["lev"]
    n_lc = 2 if n_lat % 2 == 0 else 1
    n_lo = n_lat // n_lc
    devices = np.asarray(mesh.devices).reshape(n_lo, n_lc, n_lev)
    staged_mesh = Mesh(devices, ("lo", "lc", "lev"))
    return jax.shard_map(
        make_per_device(n_lo, n_lc, n_lev),
        mesh=staged_mesh,
        in_specs=(
            P(None, LAT, "lev", None),
            P(LAT, "lev", None),
            P(LAT, "lev", None),
            P(LAT, None, None),
            P(),
            P(),
            P(),
            P(),
        ),
        out_specs=P(None, LAT, "lev", None),
        check_vma=False,
    )
```
